512 devices in a mesh: dp: 32 (over x_hi, z, core), expert: 16 (over y, x_lo).
Axes of the slice: x: 4 (x_hi: 2, x_lo: 2; x = x_hi * 2 + x_lo), y: 8, z: 8, core: 2. Of those that a mesh axis runs over, the one named last changes fastest.
Arguments:
- tokens: bfloat16 [65536, 1024], P(('dp', 'expert')), may hold values from -6 to 6
- grad_out: bfloat16 [65536, 1024], P(('dp', 'expert')), may hold values from -6 to 6
- routes: int32 [65536, 8], P(('dp', 'expert')), may hold values from 0 to 15, all different within a row; in each aligned block of 128 rows (0 to 127, 128 to 255, ...) at most 72 rows name the same one
- gates: float32 [65536, 8], P(('dp', 'expert')), may hold values from 0.1 to 1
- w_gate: bfloat16 [16, 1024, 384], P('expert', 'dp'), may hold values from -0.1875 to 0.1875
- w_up: bfloat16 [16, 1024, 384], P('expert', 'dp'), may hold values from -0.1875 to 0.1875
- w_down: bfloat16 [16, 384, 1024], P('expert', 'dp'), may hold values from -0.3125 to 0.3125
Outputs:
- grad_tokens: bfloat16 [65536, 1024], P(('dp', 'expert'))
- grad_gate: float32 [16, 1024, 384], P('expert', 'dp')
- grad_up: float32 [16, 1024, 384], P('expert', 'dp')
- grad_down: float32 [16, 384, 1024], P('expert', 'dp')
The draws below stay inside these ranges and needn't reach their ends.
Inputs may be any that keep to these rules, and one draw needn't show every extreme that they name: `routes`: each row names 8 different experts. In each aligned block of 128 rows (the rows of one device) no expert is named by more than 72 rows, and in some blocks one expert is named by exactly 72 rows.
All inputs are finite; a program needn't handle non-finite values.
Results may differ from the reference program's by a relative error of at most 0.023.
Values may be sent and summed in bfloat16 or wider, within the bound.
No kernel may reach another device: no remote copies, remote signals or barrier semaphores. Data moves between devices by JAX's collectives and lax.ppermute only.
A program may use at most 64 MiB of HBM per device.

```python
import math
import jax
import jax.numpy as jnp
import numpy as np
from jax import lax

D = 1024
H = 384
EXPERTS = 16
TOP = 8
ROWS_DEV = 128
CAP = 72
TOKENS = 65536
N_DP = 32
N_EXPERT = 16


def levels(rng, extent, cuts, least, high):
    loudness, own = 1.0, jax.random.fold_in(rng, 6)
    for position, shards_of in cuts:
        steps = jnp.exp(jax.random.uniform(jax.random.fold_in(own, position), (shards_of,), jnp.float32, least / len(cuts), high / len(cuts)))
        loudness = loudness * jnp.repeat(steps, extent[position] // shards_of).reshape([-1 if axis == position else 1 for axis in range(len(extent))])
    return loudness


def shared_out(rng, own, number, rows, number_of, top, bound, skew):
    sequence = jax.random.permutation(rng, number_of)
    crowded, common = shares(number_of, rows * top, bound, skew, True), shares(number_of, rows * top, bound, skew, False)
    places = jnp.arange(number_of)

    def named(sizes, rotation):
        used = int((sizes > 0).sum())
        fixed = max(1, used // 4)
        moved = fixed + (places - fixed + rotation * (used - fixed)) % max(1, number_of - fixed)
        return jnp.zeros((number_of,), jnp.int32).at[sequence[jnp.where(places < fixed, places, moved)]].set(jnp.asarray(sizes, jnp.int32))

    sizes = jnp.where(number % 4 == 0, named(crowded, number // 4), named(common, number - number // 4 - 1))
    mixed = jax.random.permutation(jax.random.fold_in(own, 3), number_of)
    donor, sink = mixed[0:number_of // 2 * 2:2], mixed[1:number_of // 2 * 2:2]
    slack = jnp.minimum(sizes[donor] - 1, bound - sizes[sink]) // 2
    slack = jnp.where((donor == sequence[0]) | (sink == sequence[0]) | (sizes[sink] == 0), 0, jnp.maximum(slack, 0))
    moved = jax.random.randint(jax.random.fold_in(own, 4), (number_of // 2,), 0, 1 << 20) % (slack + 1)
    sizes = sizes.at[donor].add(-moved).at[sink].add(moved)
    items = jnp.searchsorted(jnp.cumsum(sizes), jnp.arange(rows * top), side="right").astype(jnp.int32)
    table = items.reshape(top, rows).T
    table = table[jax.random.permutation(jax.random.fold_in(own, 1), rows)]
    rotation = jax.random.randint(jax.random.fold_in(own, 2), (rows, 1), 0, top)
    return jnp.take_along_axis(table, (jnp.arange(top)[None, :] + rotation) % top, axis=1)


def shares(number_of, total, limit, lean, full):
    loads = [(1 << 20) // math.isqrt(rank ** lean) + 1 for rank in range(1, number_of + 1)]
    largest = limit if full else min(limit, max(-(-total // number_of), total * loads[0] // sum(loads)))
    least = 1 if total - largest >= number_of - 1 else 0
    given, surplus = [largest] + [least] * (number_of - 1), total - largest - least * (number_of - 1)
    while surplus > 0:
        free = [i for i in range(1, number_of) if given[i] < largest] or [i for i in range(1, number_of) if given[i] < limit]
        whole, remaining = sum([loads[i] for i in free]), surplus
        for i in free:
            more = min(limit - given[i], max(1, remaining * loads[i] // whole), surplus)
            given[i] = given[i] + more
            surplus = surplus - more
    return np.array(given)


def noise(rng, dims, spread, reach, split=(), kind=jnp.bfloat16):
    drawn = jax.random.normal(rng, dims, jnp.float32) * spread
    if len(split) > 0:
        drawn = levels(rng, dims, split, -0.22, 0.18) * drawn
    return jnp.clip(drawn, min=-reach, max=reach).astype(kind)


def setup_inputs(seed: int = 0) -> dict:
    streams_of = jax.random.split(jax.random.key(seed), 8)
    tokens = noise(streams_of[0], (TOKENS, D), 1.0, 6.0, ((0, 512),))
    grad_out = noise(streams_of[1], (TOKENS, D), 1.0, 6.0, ((0, 512),))
    routes_keys = jax.random.split(jax.random.fold_in(streams_of[2], 1), TOKENS // ROWS_DEV)
    routes_turns = jax.random.permutation(jax.random.fold_in(streams_of[2], 3), TOKENS // ROWS_DEV)
    routes = jax.vmap(lambda own, number: shared_out(jax.random.fold_in(streams_of[2], 2), own, number, ROWS_DEV, EXPERTS, TOP, CAP, 1))(routes_keys, routes_turns).reshape((TOKENS, TOP))
    gates = jnp.clip(0.1 + 0.9 * jax.random.uniform(streams_of[3], (TOKENS, TOP), jnp.float32) ** levels(streams_of[3], (TOKENS, TOP), ((0, 512),), -0.2, 0.2), 0.1, 1.0)
    w_gate = noise(streams_of[4], (EXPERTS, D, H), D ** -0.5, 0.1875, ((0, 16), (1, 32)))
    w_up = noise(streams_of[5], (EXPERTS, D, H), D ** -0.5, 0.1875, ((0, 16), (1, 32)))
    w_down = noise(streams_of[6], (EXPERTS, H, D), H ** -0.5, 0.3125, ((0, 16), (1, 32)))
    return dict(tokens=tokens, grad_out=grad_out, routes=routes, gates=gates, w_gate=w_gate, w_up=w_up, w_down=w_down)


def reference(tokens, grad_out, routes, gates, w_gate, w_up, w_down):
    blocks = N_DP * N_EXPERT
    token_blocks = tokens.reshape(blocks, ROWS_DEV, D).astype(jnp.float32)
    grad_blocks = grad_out.reshape(blocks, ROWS_DEV, D).astype(jnp.float32)
    route_blocks = routes.reshape(blocks, ROWS_DEV, TOP)
    gate_blocks = gates.reshape(blocks, ROWS_DEV, TOP)
    factor = jnp.float32(TOKENS ** -0.5)
    slot_ids = jnp.arange(CAP, dtype=jnp.int32)
    high = lax.Precision.HIGHEST

    def per_expert(total, expert_id):
        matched = route_blocks == expert_id
        chosen = jnp.any(matched, axis=2).astype(jnp.int32)
        weight_sel = jnp.sum(jnp.where(matched, gate_blocks, jnp.float32(0.0)), axis=2)
        slot = jnp.cumsum(chosen, axis=1) - 1
        place = ((slot[:, None, :] == slot_ids[None, :, None]) & (chosen[:, None, :] == 1)).astype(jnp.float32)
        picked = jnp.einsum('scr,srd->scd', place, token_blocks, precision=high).astype(jnp.bfloat16)
        grad_pick = jnp.einsum('scr,srd->scd', place, grad_blocks, precision=high)
        gate_pick = jnp.einsum('scr,sr->sc', place, weight_sel, precision=high)
        scaled = (gate_pick[:, :, None] * grad_pick).astype(jnp.bfloat16)
        rows_in = picked.reshape(blocks * CAP, D)
        grads_in = scaled.reshape(blocks * CAP, D)
        gate_w = w_gate[expert_id]
        up_w = w_up[expert_id]
        down_w = w_down[expert_id]
        gate_value = jnp.dot(rows_in, gate_w, preferred_element_type=jnp.float32)
        up_value = jnp.dot(rows_in, up_w, preferred_element_type=jnp.float32)
        sigmoid_gate = jax.nn.sigmoid(gate_value)
        activated = gate_value * sigmoid_gate
        hidden = (activated * up_value).astype(jnp.bfloat16)
        d_hidden = jnp.dot(grads_in, down_w.T, preferred_element_type=jnp.float32)
        d_up = (d_hidden * activated).astype(jnp.bfloat16)
        d_gate = (d_hidden * up_value * sigmoid_gate * (1.0 + gate_value * (1.0 - sigmoid_gate))).astype(jnp.bfloat16)
        d_rows = (jnp.dot(d_gate, gate_w.T, preferred_element_type=jnp.float32)
                  + jnp.dot(d_up, up_w.T, preferred_element_type=jnp.float32)).astype(jnp.bfloat16)
        group_rows = rows_in.reshape(N_DP, N_EXPERT * CAP, D).astype(jnp.float32)
        group_hidden = hidden.reshape(N_DP, N_EXPERT * CAP, H).astype(jnp.float32)
        group_grads = grads_in.reshape(N_DP, N_EXPERT * CAP, D).astype(jnp.float32)
        group_dgate = d_gate.reshape(N_DP, N_EXPERT * CAP, H).astype(jnp.float32)
        group_dup = d_up.reshape(N_DP, N_EXPERT * CAP, H).astype(jnp.float32)
        part_gate = jnp.einsum('grd,grh->gdh', group_rows, group_dgate, precision=high).astype(jnp.bfloat16)
        part_up = jnp.einsum('grd,grh->gdh', group_rows, group_dup, precision=high).astype(jnp.bfloat16)
        part_down = jnp.einsum('grh,grd->ghd', group_hidden, group_grads, precision=high).astype(jnp.bfloat16)
        part_gate, part_up, part_down = lax.optimization_barrier((part_gate, part_up, part_down))
        gate_grad = jnp.sum(part_gate.astype(jnp.float32), axis=0) * factor
        up_grad = jnp.sum(part_up.astype(jnp.float32), axis=0) * factor
        down_grad = jnp.sum(part_down.astype(jnp.float32), axis=0) * factor
        back = d_rows.reshape(blocks, CAP, D).astype(jnp.float32)
        total = total + jnp.einsum('scr,scd->srd', place, back, precision=high)
        return total, (gate_grad, up_grad, down_grad)

    start_total = jnp.zeros((blocks, ROWS_DEV, D), jnp.float32)
    total, grads = lax.scan(per_expert, start_total, jnp.arange(EXPERTS, dtype=jnp.int32))
    grad_tokens = total.reshape(TOKENS, D).astype(jnp.bfloat16)
    return (grad_tokens, grads[0], grads[1], grads[2])
```

```python
import jax
import jax.numpy as jnp
import numpy as np
from jax import lax
from jax.sharding import Mesh
from jax.sharding import PartitionSpec as P

CAP = 72
DP = ("x_hi", "z", "core")
EX = ("y", "x_lo")


def contract_last(left, right):
    return lax.dot_general(
        left, right, (((1,), (1,)), ((), ())), preferred_element_type=jnp.float32
    )


def contract_first(left, right):
    return lax.dot_general(
        left, right, (((0,), (0,)), ((), ())), preferred_element_type=jnp.float32
    )


def make_body(n_dp, owners):
    def per_device(tokens, grad_out, routes, gates, w_gate, w_up, w_down):
        local_count = w_gate.shape[0]
        experts_all = local_count * owners
        rows_dev, dmodel = tokens.shape
        dshard, hdim = w_gate.shape[1], w_gate.shape[2]
        hshard = w_down.shape[1]
        factor = jnp.float32((rows_dev * n_dp * owners) ** (-0.5))

        down_flat = w_down[0].reshape(dshard, hdim)
        packed = jnp.stack([w_gate[0], w_up[0], down_flat])
        gathered = lax.all_gather(packed, DP, axis=0, tiled=False)
        gate_mat = gathered[:, 0].reshape(n_dp * dshard, hdim)
        up_mat = gathered[:, 1].reshape(n_dp * dshard, hdim)
        down_mat = gathered[:, 2].reshape(n_dp * hshard, dmodel)

        matched = routes[:, :, None] == jnp.arange(experts_all, dtype=jnp.int32)[None, None, :]
        chosen = jnp.any(matched, axis=1).astype(jnp.int32)
        weight_sel = jnp.sum(jnp.where(matched, gates[:, :, None], jnp.float32(0.0)), axis=1)
        slot = jnp.cumsum(chosen, axis=0) - 1
        slot_ids = jnp.arange(CAP, dtype=jnp.int32)
        place_mask = (slot.T[:, None, :] == slot_ids[None, :, None]) & (chosen.T[:, None, :] == 1)
        place_half = place_mask.astype(jnp.bfloat16)
        place_full = place_mask.astype(jnp.float32)
        picked = jnp.einsum(
            "ecr,rd->ecd", place_half, tokens, preferred_element_type=jnp.float32
        ).astype(jnp.bfloat16)
        rows_in = lax.all_to_all(picked, EX, split_axis=0, concat_axis=0, tiled=True)
        grad_pick = jnp.einsum("ecr,rd->ecd", place_half, grad_out, preferred_element_type=jnp.float32)
        gate_pick = jnp.einsum("ecr,re->ec", place_full, weight_sel, precision=lax.Precision.HIGHEST)
        scaled = (gate_pick[:, :, None] * grad_pick).astype(jnp.bfloat16)
        grads_in = lax.all_to_all(scaled, EX, split_axis=0, concat_axis=0, tiled=True)
        rows_in = rows_in.reshape(owners * CAP, dmodel)
        grads_in = grads_in.reshape(owners * CAP, dmodel)

        gate_value = jnp.dot(rows_in, gate_mat, preferred_element_type=jnp.float32)
        up_value = jnp.dot(rows_in, up_mat, preferred_element_type=jnp.float32)
        sigmoid_gate = jax.nn.sigmoid(gate_value)
        activated = gate_value * sigmoid_gate
        hidden = (activated * up_value).astype(jnp.bfloat16)
        d_hidden = contract_last(grads_in, down_mat)
        d_up = (d_hidden * activated).astype(jnp.bfloat16)
        d_gate = (
            d_hidden * up_value * sigmoid_gate * (1.0 + gate_value * (1.0 - sigmoid_gate))
        ).astype(jnp.bfloat16)
        d_rows = contract_last(d_gate, gate_mat) + contract_last(d_up, up_mat)
        back = d_rows.astype(jnp.bfloat16).reshape(owners, CAP, dmodel)
        returned = lax.all_to_all(back, EX, split_axis=0, concat_axis=0, tiled=True)

        gate_term = contract_first(rows_in, d_gate).astype(jnp.bfloat16)
        up_term = contract_first(rows_in, d_up).astype(jnp.bfloat16)
        down_term = contract_first(hidden, grads_in).astype(jnp.bfloat16)
        parts = jnp.stack(
            [
                gate_term.reshape(n_dp, dshard, hdim),
                up_term.reshape(n_dp, dshard, hdim),
                down_term.reshape(n_dp, dshard, hdim),
            ],
            axis=1,
        )
        summed = lax.psum_scatter(parts, DP, scatter_dimension=0, tiled=True)
        grad_gate = summed[:, 0].astype(jnp.float32) * factor
        grad_up = summed[:, 1].astype(jnp.float32) * factor
        grad_down = summed[:, 2].reshape(1, hshard, dmodel).astype(jnp.float32) * factor

        grad_tokens = jnp.einsum(
            "ecr,ecd->rd", place_half, returned, preferred_element_type=jnp.float32
        ).astype(jnp.bfloat16)
        return (grad_tokens, grad_gate, grad_up, grad_down)

    return per_device


def solution(mesh):
    n_dp, owners = mesh.devices.shape
    fine = Mesh(
        np.asarray(mesh.devices).reshape(2, n_dp // 4, 2, owners // 2, 2),
        ("x_hi", "z", "core", "y", "x_lo"),
    )
    rows = P(DP + EX, None)
    weights = P(EX, DP, None)
    return jax.shard_map(
        make_body(n_dp, owners),
        mesh=fine,
        in_specs=(rows, rows, rows, rows, weights, weights, weights),
        out_specs=(rows, weights, weights, weights),
        check_vma=False,
    )
```

```python
import jax
import jax.numpy as jnp
import numpy as np
from jax import lax
from jax.sharding import Mesh
from jax.sharding import PartitionSpec as P

CAP = 72
DP = ("x_hi", "z", "core")
EX = ("y", "x_lo")


def contract_last(left, right):
    return lax.dot_general(
        left, right, (((1,), (1,)), ((), ())), preferred_element_type=jnp.float32
    )


def contract_first(left, right):
    return lax.dot_general(
        left, right, (((0,), (0,)), ((), ())), preferred_element_type=jnp.float32
    )


def make_body(n_dp, owners):
    def per_device(tokens, grad_out, routes, gates, w_gate, w_up, w_down):
        local_count = w_gate.shape[0]
        experts_all = local_count * owners
        rows_dev, dmodel = tokens.shape
        dshard, hdim = w_gate.shape[1], w_gate.shape[2]
        hshard = w_down.shape[1]
        factor = jnp.float32((rows_dev * n_dp * owners) ** (-0.5))

        down_flat = w_down[0].reshape(dshard, hdim)
        packed = jnp.stack([w_gate[0], w_up[0], down_flat])[None, None, None]
        gathered = lax.all_gather(packed, "x_hi", axis=2, tiled=True)
        gathered = lax.all_gather(gathered, "z", axis=1, tiled=True)
        gathered = lax.all_gather(gathered, "core", axis=0, tiled=True)
        gathered = jnp.transpose(gathered, (2, 1, 0, 3, 4, 5))
        gathered = gathered.reshape((n_dp,) + packed.shape[3:])
        gate_mat = gathered[:, 0].reshape(n_dp * dshard, hdim)
        up_mat = gathered[:, 1].reshape(n_dp * dshard, hdim)
        down_mat = gathered[:, 2].reshape(n_dp * hshard, dmodel)

        matched = routes[:, :, None] == jnp.arange(experts_all, dtype=jnp.int32)[None, None, :]
        chosen = jnp.any(matched, axis=1).astype(jnp.int32)
        weight_sel = jnp.sum(jnp.where(matched, gates[:, :, None], jnp.float32(0.0)), axis=1)
        slot = jnp.cumsum(chosen, axis=0) - 1
        slot_ids = jnp.arange(CAP, dtype=jnp.int32)
        place_mask = (slot.T[:, None, :] == slot_ids[None, :, None]) & (chosen.T[:, None, :] == 1)
        place_half = place_mask.astype(jnp.bfloat16)
        place_full = place_mask.astype(jnp.float32)
        picked = jnp.einsum(
            "ecr,rd->ecd", place_half, tokens, preferred_element_type=jnp.float32
        ).astype(jnp.bfloat16)
        rows_in = lax.all_to_all(picked, EX, split_axis=0, concat_axis=0, tiled=True)
        grad_pick = jnp.einsum("ecr,rd->ecd", place_half, grad_out, preferred_element_type=jnp.float32)
        gate_pick = jnp.einsum("ecr,re->ec", place_full, weight_sel, precision=lax.Precision.HIGHEST)
        scaled = (gate_pick[:, :, None] * grad_pick).astype(jnp.bfloat16)
        grads_in = lax.all_to_all(scaled, EX, split_axis=0, concat_axis=0, tiled=True)
        rows_in = rows_in.reshape(owners * CAP, dmodel)
        grads_in = grads_in.reshape(owners * CAP, dmodel)

        gate_value = jnp.dot(rows_in, gate_mat, preferred_element_type=jnp.float32)
        up_value = jnp.dot(rows_in, up_mat, preferred_element_type=jnp.float32)
        sigmoid_gate = jax.nn.sigmoid(gate_value)
        activated = gate_value * sigmoid_gate
        hidden = (activated * up_value).astype(jnp.bfloat16)
        d_hidden = contract_last(grads_in, down_mat)
        d_up = (d_hidden * activated).astype(jnp.bfloat16)
        d_gate = (
            d_hidden * up_value * sigmoid_gate * (1.0 + gate_value * (1.0 - sigmoid_gate))
        ).astype(jnp.bfloat16)
        d_rows = contract_last(d_gate, gate_mat) + contract_last(d_up, up_mat)
        back = d_rows.astype(jnp.bfloat16).reshape(owners, CAP, dmodel)
        returned = lax.all_to_all(back, EX, split_axis=0, concat_axis=0, tiled=True)

        gate_term = contract_first(rows_in, d_gate).astype(jnp.bfloat16)
        up_term = contract_first(rows_in, d_up).astype(jnp.bfloat16)
        down_term = contract_first(hidden, grads_in).astype(jnp.bfloat16)
        parts = jnp.stack(
            [
                gate_term.reshape(n_dp, dshard, hdim),
                up_term.reshape(n_dp, dshard, hdim),
                down_term.reshape(n_dp, dshard, hdim),
            ],
            axis=1,
        )
        parts = parts.reshape((2, n_dp // 4, 2) + parts.shape[1:])
        parts = jnp.transpose(parts, (2, 1, 0, 3, 4, 5))
        parts = lax.psum_scatter(parts, "core", scatter_dimension=0, tiled=True)
        parts = lax.psum_scatter(parts, "z", scatter_dimension=1, tiled=True)
        parts = lax.psum_scatter(parts, "x_hi", scatter_dimension=2, tiled=True)
        summed = parts.reshape(parts.shape[2:])
        grad_gate = summed[:, 0].astype(jnp.float32) * factor
        grad_up = summed[:, 1].astype(jnp.float32) * factor
        grad_down = summed[:, 2].reshape(1, hshard, dmodel).astype(jnp.float32) * factor

        grad_tokens = jnp.einsum(
            "ecr,ecd->rd", place_half, returned, preferred_element_type=jnp.float32
        ).astype(jnp.bfloat16)
        return (grad_tokens, grad_gate, grad_up, grad_down)

    return per_device


def solution(mesh):
    n_dp, owners = mesh.devices.shape
    fine = Mesh(
        np.asarray(mesh.devices).reshape(2, n_dp // 4, 2, owners // 2, 2),
        ("x_hi", "z", "core", "y", "x_lo"),
    )
    rows = P(DP + EX, None)
    weights = P(EX, DP, None)
    return jax.shard_map(
        make_body(n_dp, owners),
        mesh=fine,
        in_specs=(rows, rows, rows, rows, weights, weights, weights),
        out_specs=(rows, weights, weights, weights),
        check_vma=False,
    )
```

```python
import jax
import jax.numpy as jnp
import numpy as np
from jax import lax
from jax.sharding import Mesh
from jax.sharding import PartitionSpec as P

CAP = 72
DP = ("x_hi", "z", "core")
EX = ("y", "x_lo")


def contract_last(left, right):
    return lax.dot_general(
        left, right, (((1,), (1,)), ((), ())), preferred_element_type=jnp.float32
    )


def contract_first(left, right):
    return lax.dot_general(
        left, right, (((0,), (0,)), ((), ())), preferred_element_type=jnp.float32
    )


def shifted(x, axis, size, step):
    perm = [(src, (src - step) % size) for src in range(size)]
    return lax.ppermute(x, axis, perm)


def gather_axis(x, axis, size):
    me = lax.axis_index(axis)
    stacked = jnp.stack([x] + [shifted(x, axis, size, k) for k in range(1, size)])
    order = (jnp.arange(size, dtype=jnp.int32) - me) % size
    return jnp.take(stacked, order, axis=0)


def scatter_sum_axis(x, axis, size):
    me = lax.axis_index(axis)
    total = lax.dynamic_index_in_dim(x, me, 0, keepdims=False).astype(jnp.float32)
    for k in range(1, size):
        piece = lax.dynamic_index_in_dim(x, (me - k) % size, 0, keepdims=False)
        total = total + shifted(piece, axis, size, k).astype(jnp.float32)
    return total


def make_body(n_dp, owners):
    def per_device(tokens, grad_out, routes, gates, w_gate, w_up, w_down):
        local_count = w_gate.shape[0]
        experts_all = local_count * owners
        rows_dev, dmodel = tokens.shape
        dshard, hdim = w_gate.shape[1], w_gate.shape[2]
        hshard = w_down.shape[1]
        factor = jnp.float32((rows_dev * n_dp * owners) ** (-0.5))

        down_flat = w_down[0].reshape(dshard, hdim)
        packed = jnp.stack([w_gate[0], w_up[0], down_flat])
        gathered = gather_axis(packed, "x_hi", 2)
        gathered = gather_axis(gathered, "z", n_dp // 4)
        gathered = gather_axis(gathered, "core", 2)
        gathered = jnp.transpose(gathered, (2, 1, 0, 3, 4, 5))
        gathered = gathered.reshape((n_dp,) + packed.shape)
        gate_mat = gathered[:, 0].reshape(n_dp * dshard, hdim)
        up_mat = gathered[:, 1].reshape(n_dp * dshard, hdim)
        down_mat = gathered[:, 2].reshape(n_dp * hshard, dmodel)

        matched = routes[:, :, None] == jnp.arange(experts_all, dtype=jnp.int32)[None, None, :]
        chosen = jnp.any(matched, axis=1).astype(jnp.int32)
        weight_sel = jnp.sum(jnp.where(matched, gates[:, :, None], jnp.float32(0.0)), axis=1)
        slot = jnp.cumsum(chosen, axis=0) - 1
        slot_ids = jnp.arange(CAP, dtype=jnp.int32)
        place_mask = (slot.T[:, None, :] == slot_ids[None, :, None]) & (chosen.T[:, None, :] == 1)
        place_half = place_mask.astype(jnp.bfloat16)
        place_full = place_mask.astype(jnp.float32)
        picked = jnp.einsum(
            "ecr,rd->ecd", place_half, tokens, preferred_element_type=jnp.float32
        ).astype(jnp.bfloat16)
        rows_in = lax.all_to_all(picked, EX, split_axis=0, concat_axis=0, tiled=True)
        grad_pick = jnp.einsum("ecr,rd->ecd", place_half, grad_out, preferred_element_type=jnp.float32)
        gate_pick = jnp.einsum("ecr,re->ec", place_full, weight_sel, precision=lax.Precision.HIGHEST)
        scaled = (gate_pick[:, :, None] * grad_pick).astype(jnp.bfloat16)
        grads_in = lax.all_to_all(scaled, EX, split_axis=0, concat_axis=0, tiled=True)
        rows_in = rows_in.reshape(owners * CAP, dmodel)
        grads_in = grads_in.reshape(owners * CAP, dmodel)

        gate_value = jnp.dot(rows_in, gate_mat, preferred_element_type=jnp.float32)
        up_value = jnp.dot(rows_in, up_mat, preferred_element_type=jnp.float32)
        sigmoid_gate = jax.nn.sigmoid(gate_value)
        activated = gate_value * sigmoid_gate
        hidden = (activated * up_value).astype(jnp.bfloat16)
        d_hidden = contract_last(grads_in, down_mat)
        d_up = (d_hidden * activated).astype(jnp.bfloat16)
        d_gate = (
            d_hidden * up_value * sigmoid_gate * (1.0 + gate_value * (1.0 - sigmoid_gate))
        ).astype(jnp.bfloat16)
        d_rows = contract_last(d_gate, gate_mat) + contract_last(d_up, up_mat)
        back = d_rows.astype(jnp.bfloat16).reshape(owners, CAP, dmodel)
        returned = lax.all_to_all(back, EX, split_axis=0, concat_axis=0, tiled=True)

        gate_term = contract_first(rows_in, d_gate).astype(jnp.bfloat16)
        up_term = contract_first(rows_in, d_up).astype(jnp.bfloat16)
        down_term = contract_first(hidden, grads_in).astype(jnp.bfloat16)
        parts = jnp.stack(
            [
                gate_term.reshape(n_dp, dshard, hdim),
                up_term.reshape(n_dp, dshard, hdim),
                down_term.reshape(n_dp, dshard, hdim),
            ],
            axis=1,
        )
        parts = parts.reshape((2, n_dp // 4, 2) + parts.shape[1:])
        parts = jnp.transpose(parts, (2, 1, 0, 3, 4, 5))
        parts = scatter_sum_axis(parts, "core", 2).astype(jnp.bfloat16)
        parts = scatter_sum_axis(parts, "z", n_dp // 4).astype(jnp.bfloat16)
        summed = scatter_sum_axis(parts, "x_hi", 2)
        grad_gate = summed[0][None] * factor
        grad_up = summed[1][None] * factor
        grad_down = summed[2].reshape(1, hshard, dmodel) * factor

        grad_tokens = jnp.einsum(
            "ecr,ecd->rd", place_half, returned, preferred_element_type=jnp.float32
        ).astype(jnp.bfloat16)
        return (grad_tokens, grad_gate, grad_up, grad_down)

    return per_device


def solution(mesh):
    n_dp, owners = mesh.devices.shape
    fine = Mesh(
        np.asarray(mesh.devices).reshape(2, n_dp // 4, 2, owners // 2, 2),
        ("x_hi", "z", "core", "y", "x_lo"),
    )
    rows = P(DP + EX, None)
    weights = P(EX, DP, None)
    return jax.shard_map(
        make_body(n_dp, owners),
        mesh=fine,
        in_specs=(rows, rows, rows, rows, weights, weights, weights),
        out_specs=(rows, weights, weights, weights),
        check_vma=False,
    )
```

```python
import jax
import jax.numpy as jnp
import numpy as np
from jax import lax
from jax.sharding import Mesh
from jax.sharding import PartitionSpec as P

CAP = 72
DP = ("x_hi", "z", "core")
EX = ("y", "x_lo")


def contract_last(left, right):
    return lax.dot_general(
        left, right, (((1,), (1,)), ((), ())), preferred_element_type=jnp.float32
    )


def contract_first(left, right):
    return lax.dot_general(
        left, right, (((0,), (0,)), ((), ())), preferred_element_type=jnp.float32
    )


def shifted(x, axis, size, step):
    perm = [(src, (src - step) % size) for src in range(size)]
    return lax.ppermute(x, axis, perm)


def gather_axis(x, axis, size):
    me = lax.axis_index(axis)
    stacked = jnp.stack([x] + [shifted(x, axis, size, k) for k in range(1, size)])
    order = (jnp.arange(size, dtype=jnp.int32) - me) % size
    return jnp.take(stacked, order, axis=0)


def scatter_sum_axis(x, axis, size):
    me = lax.axis_index(axis)
    total = lax.dynamic_index_in_dim(x, me, 0, keepdims=False).astype(jnp.float32)
    for k in range(1, size):
        piece = lax.dynamic_index_in_dim(x, (me - k) % size, 0, keepdims=False)
        total = total + shifted(piece, axis, size, k).astype(jnp.float32)
    return total


def make_body(n_dp, owners):
    def per_device(tokens, grad_out, routes, gates, w_gate, w_up, w_down):
        local_count = w_gate.shape[0]
        experts_all = local_count * owners
        rows_dev, dmodel = tokens.shape
        dshard, hdim = w_gate.shape[1], w_gate.shape[2]
        hshard = w_down.shape[1]
        factor = jnp.float32((rows_dev * n_dp * owners) ** (-0.5))

        down_flat = w_down[0].reshape(dshard, hdim)
        packed = jnp.stack([w_gate[0], w_up[0], down_flat])
        gathered = gather_axis(packed, "x_hi", 2)
        gathered = gather_axis(gathered, "z", n_dp // 4)
        gathered = gather_axis(gathered, "core", 2)
        gathered = jnp.transpose(gathered, (2, 1, 0, 3, 4, 5))
        gathered = gathered.reshape((n_dp,) + packed.shape)
        gate_mat = gathered[:, 0].reshape(n_dp * dshard, hdim)
        up_mat = gathered[:, 1].reshape(n_dp * dshard, hdim)
        down_mat = gathered[:, 2].reshape(n_dp * hshard, dmodel)

        matched = routes[:, :, None] == jnp.arange(experts_all, dtype=jnp.int32)[None, None, :]
        chosen = jnp.any(matched, axis=1).astype(jnp.int32)
        weight_sel = jnp.sum(jnp.where(matched, gates[:, :, None], jnp.float32(0.0)), axis=1)
        slot = jnp.cumsum(chosen, axis=0) - 1
        slot_ids = jnp.arange(CAP, dtype=jnp.int32)
        place_mask = (slot.T[:, None, :] == slot_ids[None, :, None]) & (chosen.T[:, None, :] == 1)
        place_half = place_mask.astype(jnp.bfloat16)
        place_full = place_mask.astype(jnp.float32)
        picked = jnp.einsum(
            "ecr,rd->ecd", place_half, tokens, preferred_element_type=jnp.float32
        ).astype(jnp.bfloat16)
        rows_in = lax.all_to_all(picked, EX, split_axis=0, concat_axis=0, tiled=True)
        grad_pick = jnp.einsum("ecr,rd->ecd", place_half, grad_out, preferred_element_type=jnp.float32)
        gate_pick = jnp.einsum("ecr,re->ec", place_full, weight_sel, precision=lax.Precision.HIGHEST)
        scaled = (gate_pick[:, :, None] * grad_pick).astype(jnp.bfloat16)
        grads_in = lax.all_to_all(scaled, EX, split_axis=0, concat_axis=0, tiled=True)
        rows_in = rows_in.reshape(owners * CAP, dmodel)
        grads_in = grads_in.reshape(owners * CAP, dmodel)

        gate_value = jnp.dot(rows_in, gate_mat, preferred_element_type=jnp.float32)
        up_value = jnp.dot(rows_in, up_mat, preferred_element_type=jnp.float32)
        sigmoid_gate = jax.nn.sigmoid(gate_value)
        activated = gate_value * sigmoid_gate
        hidden = (activated * up_value).astype(jnp.bfloat16)
        d_hidden = contract_last(grads_in, down_mat)
        d_up = (d_hidden * activated).astype(jnp.bfloat16)
        d_gate = (
            d_hidden * up_value * sigmoid_gate * (1.0 + gate_value * (1.0 - sigmoid_gate))
        ).astype(jnp.bfloat16)
        d_rows = contract_last(d_gate, gate_mat) + contract_last(d_up, up_mat)
        back = d_rows.astype(jnp.bfloat16).reshape(owners, CAP, dmodel)
        returned = lax.all_to_all(back, EX, split_axis=0, concat_axis=0, tiled=True)

        gate_term = contract_first(rows_in, d_gate).astype(jnp.bfloat16)
        up_term = contract_first(rows_in, d_up).astype(jnp.bfloat16)
        down_term = contract_first(hidden, grads_in).astype(jnp.bfloat16)
        parts = jnp.stack(
            [
                gate_term.reshape(n_dp, dshard, hdim),
                up_term.reshape(n_dp, dshard, hdim),
                down_term.reshape(n_dp, dshard, hdim),
            ],
            axis=1,
        )
        parts = parts.reshape((2, n_dp // 4, 2) + parts.shape[1:])
        parts = jnp.transpose(parts, (2, 1, 0, 3, 4, 5))
        parts = scatter_sum_axis(parts, "core", 2).astype(jnp.bfloat16)
        parts = jnp.transpose(parts, (1, 0, 2, 3, 4)).reshape((n_dp // 2,) + parts.shape[2:])
        parts = lax.psum_scatter(parts, ("x_hi", "z"), scatter_dimension=0, tiled=True)
        summed = parts[0].astype(jnp.float32)
        grad_gate = summed[0][None] * factor
        grad_up = summed[1][None] * factor
        grad_down = summed[2].reshape(1, hshard, dmodel) * factor

        grad_tokens = jnp.einsum(
            "ecr,ecd->rd", place_half, returned, preferred_element_type=jnp.float32
        ).astype(jnp.bfloat16)
        return (grad_tokens, grad_gate, grad_up, grad_down)

    return per_device


def solution(mesh):
    n_dp, owners = mesh.devices.shape
    fine = Mesh(
        np.asarray(mesh.devices).reshape(2, n_dp // 4, 2, owners // 2, 2),
        ("x_hi", "z", "core", "y", "x_lo"),
    )
    rows = P(DP + EX, None)
    weights = P(EX, DP, None)
    return jax.shard_map(
        make_body(n_dp, owners),
        mesh=fine,
        in_specs=(rows, rows, rows, rows, weights, weights, weights),
        out_specs=(rows, weights, weights, weights),
        check_vma=False,
    )
```

```python
import jax
import jax.numpy as jnp
import numpy as np
from jax import lax
from jax.sharding import Mesh
from jax.sharding import PartitionSpec as P

CAP = 72
DP = ("x_hi", "z", "core")
EX = ("y", "x_lo")


def contract_last(left, right):
    return lax.dot_general(
        left, right, (((1,), (1,)), ((), ())), preferred_element_type=jnp.float32
    )


def contract_first(left, right):
    return lax.dot_general(
        left, right, (((0,), (0,)), ((), ())), preferred_element_type=jnp.float32
    )


def shifted(x, axis, size, step):
    perm = [(src, (src - step) % size) for src in range(size)]
    return lax.ppermute(x, axis, perm)


def gather_axis(x, axis, size):
    me = lax.axis_index(axis)
    stacked = jnp.stack([x] + [shifted(x, axis, size, k) for k in range(1, size)])
    order = (jnp.arange(size, dtype=jnp.int32) - me) % size
    return jnp.take(stacked, order, axis=0)


def scatter_sum_axis(x, axis, size):
    me = lax.axis_index(axis)
    total = lax.dynamic_index_in_dim(x, me, 0, keepdims=False).astype(jnp.float32)
    for k in range(1, size):
        piece = lax.dynamic_index_in_dim(x, (me - k) % size, 0, keepdims=False)
        total = total + shifted(piece, axis, size, k).astype(jnp.float32)
    return total


def scatter_sum_paired(x, axis, size):
    me = lax.axis_index(axis)
    odd, group = me % 2, me // 2
    half = size // 2
    split = jnp.swapaxes(x.reshape((half, 2) + x.shape[1:]), 0, 1)
    mine = lax.dynamic_index_in_dim(split, odd, 0, keepdims=False).astype(jnp.float32)
    other = lax.dynamic_index_in_dim(split, 1 - odd, 0, keepdims=False)
    swapped = lax.ppermute(other, axis, [(j, j ^ 1) for j in range(size)])
    paired = (mine + swapped.astype(jnp.float32)).astype(jnp.bfloat16)
    total = lax.dynamic_index_in_dim(paired, group, 0, keepdims=False).astype(jnp.float32)
    for k in range(1, half):
        piece = lax.dynamic_index_in_dim(paired, (group - k) % half, 0, keepdims=False)
        total = total + shifted(piece, axis, size, 2 * k).astype(jnp.float32)
    return total


def make_body(n_dp, owners):
    def per_device(tokens, grad_out, routes, gates, w_gate, w_up, w_down):
        local_count = w_gate.shape[0]
        experts_all = local_count * owners
        rows_dev, dmodel = tokens.shape
        dshard, hdim = w_gate.shape[1], w_gate.shape[2]
        hshard = w_down.shape[1]
        factor = jnp.float32((rows_dev * n_dp * owners) ** (-0.5))

        down_flat = w_down[0].reshape(dshard, hdim)
        packed = jnp.stack([w_gate[0], w_up[0], down_flat])
        gathered = gather_axis(packed, "x_hi", 2)
        gathered = gather_axis(gathered, "z", n_dp // 4)
        gathered = gather_axis(gathered, "core", 2)
        gathered = jnp.transpose(gathered, (2, 1, 0, 3, 4, 5))
        gathered = gathered.reshape((n_dp,) + packed.shape)
        gate_mat = gathered[:, 0].reshape(n_dp * dshard, hdim)
        up_mat = gathered[:, 1].reshape(n_dp * dshard, hdim)
        down_mat = gathered[:, 2].reshape(n_dp * hshard, dmodel)

        matched = routes[:, :, None] == jnp.arange(experts_all, dtype=jnp.int32)[None, None, :]
        chosen = jnp.any(matched, axis=1).astype(jnp.int32)
        weight_sel = jnp.sum(jnp.where(matched, gates[:, :, None], jnp.float32(0.0)), axis=1)
        slot = jnp.cumsum(chosen, axis=0) - 1
        slot_ids = jnp.arange(CAP, dtype=jnp.int32)
        place_mask = (slot.T[:, None, :] == slot_ids[None, :, None]) & (chosen.T[:, None, :] == 1)
        place_half = place_mask.astype(jnp.bfloat16)
        place_full = place_mask.astype(jnp.float32)
        picked = jnp.einsum(
            "ecr,rd->ecd", place_half, tokens, preferred_element_type=jnp.float32
        ).astype(jnp.bfloat16)
        rows_in = lax.all_to_all(picked, EX, split_axis=0, concat_axis=0, tiled=True)
        grad_pick = jnp.einsum("ecr,rd->ecd", place_half, grad_out, preferred_element_type=jnp.float32)
        gate_pick = jnp.einsum("ecr,re->ec", place_full, weight_sel, precision=lax.Precision.HIGHEST)
        scaled = (gate_pick[:, :, None] * grad_pick).astype(jnp.bfloat16)
        grads_in = lax.all_to_all(scaled, EX, split_axis=0, concat_axis=0, tiled=True)
        rows_in = rows_in.reshape(owners * CAP, dmodel)
        grads_in = grads_in.reshape(owners * CAP, dmodel)

        gate_value = jnp.dot(rows_in, gate_mat, preferred_element_type=jnp.float32)
        up_value = jnp.dot(rows_in, up_mat, preferred_element_type=jnp.float32)
        sigmoid_gate = jax.nn.sigmoid(gate_value)
        activated = gate_value * sigmoid_gate
        hidden = (activated * up_value).astype(jnp.bfloat16)
        d_hidden = contract_last(grads_in, down_mat)
        d_up = (d_hidden * activated).astype(jnp.bfloat16)
        d_gate = (
            d_hidden * up_value * sigmoid_gate * (1.0 + gate_value * (1.0 - sigmoid_gate))
        ).astype(jnp.bfloat16)
        d_rows = contract_last(d_gate, gate_mat) + contract_last(d_up, up_mat)
        back = d_rows.astype(jnp.bfloat16).reshape(owners, CAP, dmodel)
        returned = lax.all_to_all(back, EX, split_axis=0, concat_axis=0, tiled=True)

        gate_term = contract_first(rows_in, d_gate).astype(jnp.bfloat16)
        up_term = contract_first(rows_in, d_up).astype(jnp.bfloat16)
        down_term = contract_first(hidden, grads_in).astype(jnp.bfloat16)
        parts = jnp.stack(
            [
                gate_term.reshape(n_dp, dshard, hdim),
                up_term.reshape(n_dp, dshard, hdim),
                down_term.reshape(n_dp, dshard, hdim),
            ],
            axis=1,
        )
        parts = parts.reshape((2, n_dp // 4, 2) + parts.shape[1:])
        parts = jnp.transpose(parts, (2, 1, 0, 3, 4, 5))
        parts = scatter_sum_axis(parts, "core", 2).astype(jnp.bfloat16)
        parts = scatter_sum_paired(parts, "z", n_dp // 4).astype(jnp.bfloat16)
        summed = scatter_sum_axis(parts, "x_hi", 2)
        grad_gate = summed[0][None] * factor
        grad_up = summed[1][None] * factor
        grad_down = summed[2].reshape(1, hshard, dmodel) * factor

        grad_tokens = jnp.einsum(
            "ecr,ecd->rd", place_half, returned, preferred_element_type=jnp.float32
        ).astype(jnp.bfloat16)
        return (grad_tokens, grad_gate, grad_up, grad_down)

    return per_device


def solution(mesh):
    n_dp, owners = mesh.devices.shape
    fine = Mesh(
        np.asarray(mesh.devices).reshape(2, n_dp // 4, 2, owners // 2, 2),
        ("x_hi", "z", "core", "y", "x_lo"),
    )
    rows = P(DP + EX, None)
    weights = P(EX, DP, None)
    return jax.shard_map(
        make_body(n_dp, owners),
        mesh=fine,
        in_specs=(rows, rows, rows, rows, weights, weights, weights),
        out_specs=(rows, weights, weights, weights),
        check_vma=False,
    )
```

```python
import jax
import jax.numpy as jnp
import numpy as np
from jax import lax
from jax.sharding import Mesh
from jax.sharding import PartitionSpec as P

CAP = 72
DP = ("x_hi", "z", "core")
EX = ("y", "x_lo")


def contract_last(left, right):
    return lax.dot_general(
        left, right, (((1,), (1,)), ((), ())), preferred_element_type=jnp.float32
    )


def contract_first(left, right):
    return lax.dot_general(
        left, right, (((0,), (0,)), ((), ())), preferred_element_type=jnp.float32
    )


def shifted(x, axis, size, step):
    perm = [(src, (src - step) % size) for src in range(size)]
    return lax.ppermute(x, axis, perm)


def gather_axis(x, axis, size):
    me = lax.axis_index(axis)
    stacked = jnp.stack([x] + [shifted(x, axis, size, k) for k in range(1, size)])
    order = (jnp.arange(size, dtype=jnp.int32) - me) % size
    return jnp.take(stacked, order, axis=0)


def scatter_sum_axis(x, axis, size):
    me = lax.axis_index(axis)
    total = lax.dynamic_index_in_dim(x, me, 0, keepdims=False).astype(jnp.float32)
    for k in range(1, size):
        piece = lax.dynamic_index_in_dim(x, (me - k) % size, 0, keepdims=False)
        total = total + shifted(piece, axis, size, k).astype(jnp.float32)
    return total


def scatter_sum_paired(x, axis, size):
    me = lax.axis_index(axis)
    odd, group = me % 2, me // 2
    half = size // 2
    split = jnp.swapaxes(x.reshape((half, 2) + x.shape[1:]), 0, 1)
    mine = lax.dynamic_index_in_dim(split, odd, 0, keepdims=False).astype(jnp.float32)
    other = lax.dynamic_index_in_dim(split, 1 - odd, 0, keepdims=False)
    swapped = lax.ppermute(other, axis, [(j, j ^ 1) for j in range(size)])
    paired = (mine + swapped.astype(jnp.float32)).astype(jnp.bfloat16)
    total = lax.dynamic_index_in_dim(paired, group, 0, keepdims=False).astype(jnp.float32)
    for k in range(1, half):
        piece = lax.dynamic_index_in_dim(paired, (group - k) % half, 0, keepdims=False)
        total = total + shifted(piece, axis, size, 2 * k).astype(jnp.float32)
    return total


def make_body(n_dp, owners):
    def per_device(tokens, grad_out, routes, gates, w_gate, w_up, w_down):
        local_count = w_gate.shape[0]
        experts_all = local_count * owners
        rows_dev, dmodel = tokens.shape
        dshard, hdim = w_gate.shape[1], w_gate.shape[2]
        hshard = w_down.shape[1]
        factor = jnp.float32((rows_dev * n_dp * owners) ** (-0.5))

        down_flat = w_down[0].reshape(dshard, hdim)
        packed = jnp.stack([w_gate[0], w_up[0], down_flat])
        gathered = gather_axis(packed, "x_hi", 2)
        gathered = gather_axis(gathered, "z", n_dp // 4)
        gathered = gather_axis(gathered, "core", 2)
        gathered = jnp.transpose(gathered, (2, 1, 0, 3, 4, 5))
        gathered = gathered.reshape((n_dp,) + packed.shape)
        gate_mat = gathered[:, 0].reshape(n_dp * dshard, hdim)
        up_mat = gathered[:, 1].reshape(n_dp * dshard, hdim)
        down_mat = gathered[:, 2].reshape(n_dp * hshard, dmodel)

        matched = routes[:, :, None] == jnp.arange(experts_all, dtype=jnp.int32)[None, None, :]
        chosen = jnp.any(matched, axis=1).astype(jnp.int32)
        weight_sel = jnp.sum(jnp.where(matched, gates[:, :, None], jnp.float32(0.0)), axis=1)
        slot = jnp.cumsum(chosen, axis=0) - 1
        slot_ids = jnp.arange(CAP, dtype=jnp.int32)
        place_mask = (slot.T[:, None, :] == slot_ids[None, :, None]) & (chosen.T[:, None, :] == 1)
        place_half = place_mask.astype(jnp.bfloat16)
        place_full = place_mask.astype(jnp.float32)
        picked = jnp.einsum(
            "ecr,rd->ecd", place_half, tokens, preferred_element_type=jnp.float32
        ).astype(jnp.bfloat16)
        grad_pick = jnp.einsum("ecr,rd->ecd", place_half, grad_out, preferred_element_type=jnp.float32)
        gate_pick = jnp.einsum("ecr,re->ec", place_full, weight_sel, precision=lax.Precision.HIGHEST)
        scaled = (gate_pick[:, :, None] * grad_pick).astype(jnp.bfloat16)
        both = lax.all_to_all(
            jnp.concatenate([picked, scaled], axis=2), EX, split_axis=0, concat_axis=0, tiled=True
        )
        rows_in = both[:, :, :dmodel].reshape(owners * CAP, dmodel)
        grads_in = both[:, :, dmodel:].reshape(owners * CAP, dmodel)

        gate_value = jnp.dot(rows_in, gate_mat, preferred_element_type=jnp.float32)
        up_value = jnp.dot(rows_in, up_mat, preferred_element_type=jnp.float32)
        sigmoid_gate = jax.nn.sigmoid(gate_value)
        activated = gate_value * sigmoid_gate
        hidden = (activated * up_value).astype(jnp.bfloat16)
        d_hidden = contract_last(grads_in, down_mat)
        d_up = (d_hidden * activated).astype(jnp.bfloat16)
        d_gate = (
            d_hidden * up_value * sigmoid_gate * (1.0 + gate_value * (1.0 - sigmoid_gate))
        ).astype(jnp.bfloat16)
        d_rows = contract_last(d_gate, gate_mat) + contract_last(d_up, up_mat)
        back = d_rows.astype(jnp.bfloat16).reshape(owners, CAP, dmodel)
        returned = lax.all_to_all(back, EX, split_axis=0, concat_axis=0, tiled=True)

        gate_term = contract_first(rows_in, d_gate).astype(jnp.bfloat16)
        up_term = contract_first(rows_in, d_up).astype(jnp.bfloat16)
        down_term = contract_first(hidden, grads_in).astype(jnp.bfloat16)
        parts = jnp.stack(
            [
                gate_term.reshape(n_dp, dshard, hdim),
                up_term.reshape(n_dp, dshard, hdim),
                down_term.reshape(n_dp, dshard, hdim),
            ],
            axis=1,
        )
        parts = parts.reshape((2, n_dp // 4, 2) + parts.shape[1:])
        parts = jnp.transpose(parts, (2, 1, 0, 3, 4, 5))
        parts = scatter_sum_axis(parts, "core", 2).astype(jnp.bfloat16)
        parts = scatter_sum_paired(parts, "z", n_dp // 4).astype(jnp.bfloat16)
        summed = scatter_sum_axis(parts, "x_hi", 2)
        grad_gate = summed[0][None] * factor
        grad_up = summed[1][None] * factor
        grad_down = summed[2].reshape(1, hshard, dmodel) * factor

        grad_tokens = jnp.einsum(
            "ecr,ecd->rd", place_half, returned, preferred_element_type=jnp.float32
        ).astype(jnp.bfloat16)
        return (grad_tokens, grad_gate, grad_up, grad_down)

    return per_device


def solution(mesh):
    n_dp, owners = mesh.devices.shape
    fine = Mesh(
        np.asarray(mesh.devices).reshape(2, n_dp // 4, 2, owners // 2, 2),
        ("x_hi", "z", "core", "y", "x_lo"),
    )
    rows = P(DP + EX, None)
    weights = P(EX, DP, None)
    return jax.shard_map(
        make_body(n_dp, owners),
        mesh=fine,
        in_specs=(rows, rows, rows, rows, weights, weights, weights),
        out_specs=(rows, weights, weights, weights),
        check_vma=False,
    )
```

```python
import jax
import jax.numpy as jnp
import numpy as np
from jax import lax
from jax.sharding import Mesh
from jax.sharding import PartitionSpec as P

CAP = 72
DP = ("x_hi", "z", "core")
EX = ("y", "x_lo")


def contract_last(left, right):
    return lax.dot_general(
        left, right, (((1,), (1,)), ((), ())), preferred_element_type=jnp.float32
    )


def contract_first(left, right):
    return lax.dot_general(
        left, right, (((0,), (0,)), ((), ())), preferred_element_type=jnp.float32
    )


def shifted(x, axis, size, step):
    perm = [(src, (src - step) % size) for src in range(size)]
    return lax.ppermute(x, axis, perm)


def gather_axis(x, axis, size):
    me = lax.axis_index(axis)
    stacked = jnp.stack([x] + [shifted(x, axis, size, k) for k in range(1, size)])
    order = (jnp.arange(size, dtype=jnp.int32) - me) % size
    return jnp.take(stacked, order, axis=0)


def scatter_sum_axis(x, axis, size):
    me = lax.axis_index(axis)
    total = lax.dynamic_index_in_dim(x, me, 0, keepdims=False).astype(jnp.float32)
    for k in range(1, size):
        piece = lax.dynamic_index_in_dim(x, (me - k) % size, 0, keepdims=False)
        total = total + shifted(piece, axis, size, k).astype(jnp.float32)
    return total


def scatter_sum_paired(x, axis, size):
    me = lax.axis_index(axis)
    odd, group = me % 2, me // 2
    half = size // 2
    split = jnp.swapaxes(x.reshape((half, 2) + x.shape[1:]), 0, 1)
    mine = lax.dynamic_index_in_dim(split, odd, 0, keepdims=False).astype(jnp.float32)
    other = lax.dynamic_index_in_dim(split, 1 - odd, 0, keepdims=False)
    swapped = lax.ppermute(other, axis, [(j, j ^ 1) for j in range(size)])
    paired = (mine + swapped.astype(jnp.float32)).astype(jnp.bfloat16)
    total = lax.dynamic_index_in_dim(paired, group, 0, keepdims=False).astype(jnp.float32)
    for k in range(1, half):
        piece = lax.dynamic_index_in_dim(paired, (group - k) % half, 0, keepdims=False)
        total = total + shifted(piece, axis, size, 2 * k).astype(jnp.float32)
    return total


def make_body(n_dp, owners):
    def per_device(tokens, grad_out, routes, gates, w_gate, w_up, w_down):
        local_count = w_gate.shape[0]
        experts_all = local_count * owners
        rows_dev, dmodel = tokens.shape
        dshard, hdim = w_gate.shape[1], w_gate.shape[2]
        hshard = w_down.shape[1]
        factor = jnp.float32((rows_dev * n_dp * owners) ** (-0.5))

        down_flat = w_down[0].reshape(dshard, hdim)
        packed = jnp.stack([w_gate[0], w_up[0], down_flat])
        gathered = gather_axis(packed, "x_hi", 2)
        gathered = gather_axis(gathered, "z", n_dp // 4)
        gathered = gather_axis(gathered, "core", 2)
        gathered = jnp.transpose(gathered, (2, 1, 0, 3, 4, 5))
        gathered = gathered.reshape((n_dp,) + packed.shape)
        gate_mat = gathered[:, 0].reshape(n_dp * dshard, hdim)
        up_mat = gathered[:, 1].reshape(n_dp * dshard, hdim)
        down_mat = gathered[:, 2].reshape(n_dp * hshard, dmodel)

        matched = routes[:, :, None] == jnp.arange(experts_all, dtype=jnp.int32)[None, None, :]
        chosen = jnp.any(matched, axis=1).astype(jnp.int32)
        weight_sel = jnp.sum(jnp.where(matched, gates[:, :, None], jnp.float32(0.0)), axis=1)
        slot = jnp.cumsum(chosen, axis=0) - 1
        slot_ids = jnp.arange(CAP, dtype=jnp.int32)
        place_mask = (slot.T[:, None, :] == slot_ids[None, :, None]) & (chosen.T[:, None, :] == 1)
        place_half = place_mask.astype(jnp.bfloat16)
        place_full = place_mask.astype(jnp.float32)
        picked = jnp.einsum(
            "ecr,rd->ecd", place_half, tokens, preferred_element_type=jnp.float32
        ).astype(jnp.bfloat16)
        grad_pick = jnp.einsum("ecr,rd->ecd", place_half, grad_out, preferred_element_type=jnp.float32)
        gate_pick = jnp.einsum("ecr,re->ec", place_full, weight_sel, precision=lax.Precision.HIGHEST)
        scaled = (gate_pick[:, :, None] * grad_pick).astype(jnp.bfloat16)
        both = lax.all_to_all(
            jnp.concatenate([picked, scaled], axis=2), EX, split_axis=0, concat_axis=0, tiled=True
        )
        rows_in = both[:, :, :dmodel].reshape(owners * CAP, dmodel)
        grads_in = both[:, :, dmodel:].reshape(owners * CAP, dmodel)

        gate_value = jnp.dot(rows_in, gate_mat, preferred_element_type=jnp.float32)
        up_value = jnp.dot(rows_in, up_mat, preferred_element_type=jnp.float32)
        sigmoid_gate = jax.nn.sigmoid(gate_value)
        activated = gate_value * sigmoid_gate
        hidden = (activated * up_value).astype(jnp.bfloat16)
        d_hidden = contract_last(grads_in, down_mat)
        d_up = (d_hidden * activated).astype(jnp.bfloat16)
        d_gate = (
            d_hidden * up_value * sigmoid_gate * (1.0 + gate_value * (1.0 - sigmoid_gate))
        ).astype(jnp.bfloat16)

        gate_term = contract_first(rows_in, d_gate).astype(jnp.bfloat16)
        up_term = contract_first(rows_in, d_up).astype(jnp.bfloat16)
        down_term = contract_first(hidden, grads_in).astype(jnp.bfloat16)
        parts = jnp.stack(
            [
                gate_term.reshape(n_dp, dshard, hdim),
                up_term.reshape(n_dp, dshard, hdim),
                down_term.reshape(n_dp, dshard, hdim),
            ],
            axis=1,
        )
        parts = parts.reshape((2, n_dp // 4, 2) + parts.shape[1:])
        parts = jnp.transpose(parts, (2, 1, 0, 3, 4, 5))
        parts = scatter_sum_axis(parts, "core", 2).astype(jnp.bfloat16)
        parts, d_gate, d_up = lax.optimization_barrier((parts, d_gate, d_up))
        d_rows = contract_last(d_gate, gate_mat) + contract_last(d_up, up_mat)
        back = d_rows.astype(jnp.bfloat16).reshape(owners, CAP, dmodel)
        returned = lax.all_to_all(back, EX, split_axis=0, concat_axis=0, tiled=True)
        parts = scatter_sum_paired(parts, "z", n_dp // 4).astype(jnp.bfloat16)
        summed = scatter_sum_axis(parts, "x_hi", 2)
        grad_gate = summed[0][None] * factor
        grad_up = summed[1][None] * factor
        grad_down = summed[2].reshape(1, hshard, dmodel) * factor

        grad_tokens = jnp.einsum(
            "ecr,ecd->rd", place_half, returned, preferred_element_type=jnp.float32
        ).astype(jnp.bfloat16)
        return (grad_tokens, grad_gate, grad_up, grad_down)

    return per_device


def solution(mesh):
    n_dp, owners = mesh.devices.shape
    fine = Mesh(
        np.asarray(mesh.devices).reshape(2, n_dp // 4, 2, owners // 2, 2),
        ("x_hi", "z", "core", "y", "x_lo"),
    )
    rows = P(DP + EX, None)
    weights = P(EX, DP, None)
    return jax.shard_map(
        make_body(n_dp, owners),
        mesh=fine,
        in_specs=(rows, rows, rows, rows, weights, weights, weights),
        out_specs=(rows, weights, weights, weights),
        check_vma=False,
    )
```

```python
import jax
import jax.numpy as jnp
import numpy as np
from jax import lax
from jax.sharding import Mesh
from jax.sharding import PartitionSpec as P

CAP = 72
DP = ("x_hi", "z", "core")
EX = ("y", "x_lo")


def contract_last(left, right):
    return lax.dot_general(
        left, right, (((1,), (1,)), ((), ())), preferred_element_type=jnp.float32
    )


def contract_first(left, right):
    return lax.dot_general(
        left, right, (((0,), (0,)), ((), ())), preferred_element_type=jnp.float32
    )


def shifted(x, axis, size, step):
    perm = [(src, (src - step) % size) for src in range(size)]
    return lax.ppermute(x, axis, perm)


def gather_axis(x, axis, size):
    me = lax.axis_index(axis)
    stacked = jnp.stack([x] + [shifted(x, axis, size, k) for k in range(1, size)])
    order = (jnp.arange(size, dtype=jnp.int32) - me) % size
    return jnp.take(stacked, order, axis=0)


def scatter_sum_axis(x, axis, size):
    me = lax.axis_index(axis)
    total = lax.dynamic_index_in_dim(x, me, 0, keepdims=False).astype(jnp.float32)
    for k in range(1, size):
        piece = lax.dynamic_index_in_dim(x, (me - k) % size, 0, keepdims=False)
        total = total + shifted(piece, axis, size, k).astype(jnp.float32)
    return total


def scatter_sum_paired(x, axis, size):
    me = lax.axis_index(axis)
    odd, group = me % 2, me // 2
    half = size // 2
    split = jnp.swapaxes(x.reshape((half, 2) + x.shape[1:]), 0, 1)
    mine = lax.dynamic_index_in_dim(split, odd, 0, keepdims=False).astype(jnp.float32)
    other = lax.dynamic_index_in_dim(split, 1 - odd, 0, keepdims=False)
    swapped = lax.ppermute(other, axis, [(j, j ^ 1) for j in range(size)])
    paired = (mine + swapped.astype(jnp.float32)).astype(jnp.bfloat16)
    total = lax.dynamic_index_in_dim(paired, group, 0, keepdims=False).astype(jnp.float32)
    for k in range(1, half):
        piece = lax.dynamic_index_in_dim(paired, (group - k) % half, 0, keepdims=False)
        total = total + shifted(piece, axis, size, 2 * k).astype(jnp.float32)
    return total


def scatter_sum_quad(x, zsize):
    zi, xi = lax.axis_index("z"), lax.axis_index("x_hi")
    odd, group = zi % 2, zi // 2
    half = zsize // 2
    four = x.reshape((half, 4) + x.shape[2:])
    total = lax.dynamic_index_in_dim(four, odd * 2 + xi, 1, keepdims=False).astype(jnp.float32)
    for flip_b, flip_x in ((1, 0), (0, 1), (1, 1)):
        other = jnp.where(flip_b == 1, 1 - odd, odd) * 2 + jnp.where(flip_x == 1, 1 - xi, xi)
        piece = lax.dynamic_index_in_dim(four, other, 1, keepdims=False)
        perm = [
            (xh * zsize + z, (xh ^ flip_x) * zsize + (z ^ flip_b))
            for xh in range(2)
            for z in range(zsize)
        ]
        total = total + lax.ppermute(piece, ("x_hi", "z"), perm).astype(jnp.float32)
    paired = total.astype(jnp.bfloat16)
    total = lax.dynamic_index_in_dim(paired, group, 0, keepdims=False).astype(jnp.float32)
    for k in range(1, half):
        piece = lax.dynamic_index_in_dim(paired, (group - k) % half, 0, keepdims=False)
        total = total + shifted(piece, "z", zsize, 2 * k).astype(jnp.float32)
    return total


def make_body(n_dp, owners):
    def per_device(tokens, grad_out, routes, gates, w_gate, w_up, w_down):
        local_count = w_gate.shape[0]
        experts_all = local_count * owners
        rows_dev, dmodel = tokens.shape
        dshard, hdim = w_gate.shape[1], w_gate.shape[2]
        hshard = w_down.shape[1]
        factor = jnp.float32((rows_dev * n_dp * owners) ** (-0.5))

        down_flat = w_down[0].reshape(dshard, hdim)
        packed = jnp.stack([w_gate[0], w_up[0], down_flat])
        gathered = gather_axis(packed, "x_hi", 2)
        gathered = gather_axis(gathered, "z", n_dp // 4)
        gathered = gather_axis(gathered, "core", 2)
        gathered = jnp.transpose(gathered, (2, 1, 0, 3, 4, 5))
        gathered = gathered.reshape((n_dp,) + packed.shape)
        gate_mat = gathered[:, 0].reshape(n_dp * dshard, hdim)
        up_mat = gathered[:, 1].reshape(n_dp * dshard, hdim)
        down_mat = gathered[:, 2].reshape(n_dp * hshard, dmodel)

        matched = routes[:, :, None] == jnp.arange(experts_all, dtype=jnp.int32)[None, None, :]
        chosen = jnp.any(matched, axis=1).astype(jnp.int32)
        weight_sel = jnp.sum(jnp.where(matched, gates[:, :, None], jnp.float32(0.0)), axis=1)
        slot = jnp.cumsum(chosen, axis=0) - 1
        slot_ids = jnp.arange(CAP, dtype=jnp.int32)
        place_mask = (slot.T[:, None, :] == slot_ids[None, :, None]) & (chosen.T[:, None, :] == 1)
        place_half = place_mask.astype(jnp.bfloat16)
        place_full = place_mask.astype(jnp.float32)
        picked = jnp.einsum(
            "ecr,rd->ecd", place_half, tokens, preferred_element_type=jnp.float32
        ).astype(jnp.bfloat16)
        grad_pick = jnp.einsum("ecr,rd->ecd", place_half, grad_out, preferred_element_type=jnp.float32)
        gate_pick = jnp.einsum("ecr,re->ec", place_full, weight_sel, precision=lax.Precision.HIGHEST)
        scaled = (gate_pick[:, :, None] * grad_pick).astype(jnp.bfloat16)
        both = lax.all_to_all(
            jnp.concatenate([picked, scaled], axis=2), EX, split_axis=0, concat_axis=0, tiled=True
        )
        rows_in = both[:, :, :dmodel].reshape(owners * CAP, dmodel)
        grads_in = both[:, :, dmodel:].reshape(owners * CAP, dmodel)

        gate_value = jnp.dot(rows_in, gate_mat, preferred_element_type=jnp.float32)
        up_value = jnp.dot(rows_in, up_mat, preferred_element_type=jnp.float32)
        sigmoid_gate = jax.nn.sigmoid(gate_value)
        activated = gate_value * sigmoid_gate
        hidden = (activated * up_value).astype(jnp.bfloat16)
        d_hidden = contract_last(grads_in, down_mat)
        d_up = (d_hidden * activated).astype(jnp.bfloat16)
        d_gate = (
            d_hidden * up_value * sigmoid_gate * (1.0 + gate_value * (1.0 - sigmoid_gate))
        ).astype(jnp.bfloat16)

        gate_term = contract_first(rows_in, d_gate).astype(jnp.bfloat16)
        up_term = contract_first(rows_in, d_up).astype(jnp.bfloat16)
        down_term = contract_first(hidden, grads_in).astype(jnp.bfloat16)
        parts = jnp.stack(
            [
                gate_term.reshape(n_dp, dshard, hdim),
                up_term.reshape(n_dp, dshard, hdim),
                down_term.reshape(n_dp, dshard, hdim),
            ],
            axis=1,
        )
        parts = parts.reshape((2, n_dp // 4, 2) + parts.shape[1:])
        parts = jnp.transpose(parts, (2, 1, 0, 3, 4, 5))
        parts = scatter_sum_axis(parts, "core", 2).astype(jnp.bfloat16)
        parts, d_gate, d_up = lax.optimization_barrier((parts, d_gate, d_up))
        d_rows = contract_last(d_gate, gate_mat) + contract_last(d_up, up_mat)
        back = d_rows.astype(jnp.bfloat16).reshape(owners, CAP, dmodel)
        returned = lax.all_to_all(back, EX, split_axis=0, concat_axis=0, tiled=True)
        summed = scatter_sum_quad(parts, n_dp // 4)
        grad_gate = summed[0][None] * factor
        grad_up = summed[1][None] * factor
        grad_down = summed[2].reshape(1, hshard, dmodel) * factor

        grad_tokens = jnp.einsum(
            "ecr,ecd->rd", place_half, returned, preferred_element_type=jnp.float32
        ).astype(jnp.bfloat16)
        return (grad_tokens, grad_gate, grad_up, grad_down)

    return per_device


def solution(mesh):
    n_dp, owners = mesh.devices.shape
    fine = Mesh(
        np.asarray(mesh.devices).reshape(2, n_dp // 4, 2, owners // 2, 2),
        ("x_hi", "z", "core", "y", "x_lo"),
    )
    rows = P(DP + EX, None)
    weights = P(EX, DP, None)
    return jax.shard_map(
        make_body(n_dp, owners),
        mesh=fine,
        in_specs=(rows, rows, rows, rows, weights, weights, weights),
        out_specs=(rows, weights, weights, weights),
        check_vma=False,
    )
```

```python
import jax
import jax.numpy as jnp
import numpy as np
from jax import lax
from jax.sharding import Mesh
from jax.sharding import PartitionSpec as P

CAP = 72
DP = ("x_hi", "z", "core")
EX = ("y", "x_lo")


def contract_last(left, right):
    return lax.dot_general(
        left, right, (((1,), (1,)), ((), ())), preferred_element_type=jnp.float32
    )


def contract_first(left, right):
    return lax.dot_general(
        left, right, (((0,), (0,)), ((), ())), preferred_element_type=jnp.float32
    )


def shifted(x, axis, size, step):
    perm = [(src, (src - step) % size) for src in range(size)]
    return lax.ppermute(x, axis, perm)


def gather_axis(x, axis, size):
    me = lax.axis_index(axis)
    stacked = jnp.stack([x] + [shifted(x, axis, size, k) for k in range(1, size)])
    order = (jnp.arange(size, dtype=jnp.int32) - me) % size
    return jnp.take(stacked, order, axis=0)


def scatter_sum_axis(x, axis, size):
    me = lax.axis_index(axis)
    total = lax.dynamic_index_in_dim(x, me, 0, keepdims=False).astype(jnp.float32)
    for k in range(1, size):
        piece = lax.dynamic_index_in_dim(x, (me - k) % size, 0, keepdims=False)
        total = total + shifted(piece, axis, size, k).astype(jnp.float32)
    return total


def scatter_sum_paired(x, axis, size):
    me = lax.axis_index(axis)
    odd, group = me % 2, me // 2
    half = size // 2
    split = jnp.swapaxes(x.reshape((half, 2) + x.shape[1:]), 0, 1)
    mine = lax.dynamic_index_in_dim(split, odd, 0, keepdims=False).astype(jnp.float32)
    other = lax.dynamic_index_in_dim(split, 1 - odd, 0, keepdims=False)
    swapped = lax.ppermute(other, axis, [(j, j ^ 1) for j in range(size)])
    paired = (mine + swapped.astype(jnp.float32)).astype(jnp.bfloat16)
    total = lax.dynamic_index_in_dim(paired, group, 0, keepdims=False).astype(jnp.float32)
    for k in range(1, half):
        piece = lax.dynamic_index_in_dim(paired, (group - k) % half, 0, keepdims=False)
        total = total + shifted(piece, axis, size, 2 * k).astype(jnp.float32)
    return total


def scatter_sum_quad(x, zsize):
    zi, xi = lax.axis_index("z"), lax.axis_index("x_hi")
    odd, group = zi % 2, zi // 2
    half = zsize // 2
    four = x.reshape((half, 4) + x.shape[2:])
    total = lax.dynamic_index_in_dim(four, odd * 2 + xi, 1, keepdims=False).astype(jnp.float32)
    for flip_b, flip_x in ((1, 0), (0, 1), (1, 1)):
        other = jnp.where(flip_b == 1, 1 - odd, odd) * 2 + jnp.where(flip_x == 1, 1 - xi, xi)
        piece = lax.dynamic_index_in_dim(four, other, 1, keepdims=False)
        perm = [
            (xh * zsize + z, (xh ^ flip_x) * zsize + (z ^ flip_b))
            for xh in range(2)
            for z in range(zsize)
        ]
        total = total + lax.ppermute(piece, ("x_hi", "z"), perm).astype(jnp.float32)
    paired = total.astype(jnp.bfloat16)
    total = lax.dynamic_index_in_dim(paired, group, 0, keepdims=False).astype(jnp.float32)
    for k in range(1, half):
        piece = lax.dynamic_index_in_dim(paired, (group - k) % half, 0, keepdims=False)
        total = total + shifted(piece, "z", zsize, 2 * k).astype(jnp.float32)
    return total


def make_body(n_dp, owners):
    def per_device(tokens, grad_out, routes, gates, w_gate, w_up, w_down):
        local_count = w_gate.shape[0]
        experts_all = local_count * owners
        rows_dev, dmodel = tokens.shape
        dshard, hdim = w_gate.shape[1], w_gate.shape[2]
        hshard = w_down.shape[1]
        factor = jnp.float32((rows_dev * n_dp * owners) ** (-0.5))

        down_flat = w_down[0].reshape(dshard, hdim)
        packed = jnp.stack([w_gate[0], w_up[0], down_flat])
        gathered = gather_axis(packed, "x_hi", 2)
        gathered = gather_axis(gathered, "z", n_dp // 4)
        gathered = gather_axis(gathered, "core", 2)
        gathered = jnp.transpose(gathered, (2, 1, 0, 3, 4, 5))
        gathered = gathered.reshape((n_dp,) + packed.shape)
        gate_mat = gathered[:, 0].reshape(n_dp * dshard, hdim)
        up_mat = gathered[:, 1].reshape(n_dp * dshard, hdim)
        down_mat = gathered[:, 2].reshape(n_dp * hshard, dmodel)

        matched = routes[:, :, None] == jnp.arange(experts_all, dtype=jnp.int32)[None, None, :]
        chosen = jnp.any(matched, axis=1).astype(jnp.int32)
        weight_sel = jnp.sum(jnp.where(matched, gates[:, :, None], jnp.float32(0.0)), axis=1)
        slot = jnp.cumsum(chosen, axis=0) - 1
        slot_ids = jnp.arange(CAP, dtype=jnp.int32)
        place_mask = (slot.T[:, None, :] == slot_ids[None, :, None]) & (chosen.T[:, None, :] == 1)
        place_half = place_mask.astype(jnp.bfloat16)
        place_full = place_mask.astype(jnp.float32)
        picked = jnp.einsum(
            "ecr,rd->ecd", place_half, tokens, preferred_element_type=jnp.float32
        ).astype(jnp.bfloat16)
        grad_pick = jnp.einsum("ecr,rd->ecd", place_half, grad_out, preferred_element_type=jnp.float32)
        gate_pick = jnp.einsum("ecr,re->ec", place_full, weight_sel, precision=lax.Precision.HIGHEST)
        scaled = (gate_pick[:, :, None] * grad_pick).astype(jnp.bfloat16)
        both = lax.all_to_all(
            jnp.concatenate([picked, scaled], axis=2), EX, split_axis=0, concat_axis=0, tiled=True
        )
        rows_in = both[:, :, :dmodel].reshape(owners * CAP, dmodel)
        grads_in = both[:, :, dmodel:].reshape(owners * CAP, dmodel)

        gate_value = jnp.dot(rows_in, gate_mat, preferred_element_type=jnp.float32)
        up_value = jnp.dot(rows_in, up_mat, preferred_element_type=jnp.float32)
        sigmoid_gate = jax.nn.sigmoid(gate_value)
        activated = gate_value * sigmoid_gate
        hidden = (activated * up_value).astype(jnp.bfloat16)
        d_hidden = contract_last(grads_in, down_mat)
        d_up = (d_hidden * activated).astype(jnp.bfloat16)
        d_gate = (
            d_hidden * up_value * sigmoid_gate * (1.0 + gate_value * (1.0 - sigmoid_gate))
        ).astype(jnp.bfloat16)

        gate_term = contract_first(rows_in, d_gate).astype(jnp.bfloat16)
        up_term = contract_first(rows_in, d_up).astype(jnp.bfloat16)
        down_term = contract_first(hidden, grads_in).astype(jnp.bfloat16)
        parts = jnp.stack(
            [
                gate_term.reshape(n_dp, dshard, hdim),
                up_term.reshape(n_dp, dshard, hdim),
                down_term.reshape(n_dp, dshard, hdim),
            ],
            axis=1,
        )
        parts = parts.reshape((2, n_dp // 4, 2) + parts.shape[1:])
        parts = jnp.transpose(parts, (2, 1, 0, 3, 4, 5))
        parts = scatter_sum_axis(parts, "core", 2).astype(jnp.bfloat16)
        d_rows = contract_last(d_gate, gate_mat) + contract_last(d_up, up_mat)
        back = d_rows.astype(jnp.bfloat16).reshape(owners, CAP, dmodel)
        parts, back = lax.optimization_barrier((parts, back))
        returned = lax.all_to_all(back, EX, split_axis=0, concat_axis=0, tiled=True)
        summed = scatter_sum_quad(parts, n_dp // 4)
        grad_gate = summed[0][None] * factor
        grad_up = summed[1][None] * factor
        grad_down = summed[2].reshape(1, hshard, dmodel) * factor

        grad_tokens = jnp.einsum(
            "ecr,ecd->rd", place_half, returned, preferred_element_type=jnp.float32
        ).astype(jnp.bfloat16)
        return (grad_tokens, grad_gate, grad_up, grad_down)

    return per_device


def solution(mesh):
    n_dp, owners = mesh.devices.shape
    fine = Mesh(
        np.asarray(mesh.devices).reshape(2, n_dp // 4, 2, owners // 2, 2),
        ("x_hi", "z", "core", "y", "x_lo"),
    )
    rows = P(DP + EX, None)
    weights = P(EX, DP, None)
    return jax.shard_map(
        make_body(n_dp, owners),
        mesh=fine,
        in_specs=(rows, rows, rows, rows, weights, weights, weights),
        out_specs=(rows, weights, weights, weights),
        check_vma=False,
    )
```

```python
import jax
import jax.numpy as jnp
import numpy as np
from jax import lax
from jax.sharding import Mesh
from jax.sharding import PartitionSpec as P

CAP = 72
DP = ("x_hi", "z", "core")
EX = ("y", "x_lo")


def contract_last(left, right):
    return lax.dot_general(
        left, right, (((1,), (1,)), ((), ())), preferred_element_type=jnp.float32
    )


def contract_first(left, right):
    return lax.dot_general(
        left, right, (((0,), (0,)), ((), ())), preferred_element_type=jnp.float32
    )


def shifted(x, axis, size, step):
    perm = [(src, (src - step) % size) for src in range(size)]
    return lax.ppermute(x, axis, perm)


def gather_axis(x, axis, size):
    me = lax.axis_index(axis)
    stacked = jnp.stack([x] + [shifted(x, axis, size, k) for k in range(1, size)])
    order = (jnp.arange(size, dtype=jnp.int32) - me) % size
    return jnp.take(stacked, order, axis=0)


def scatter_sum_axis(x, axis, size):
    me = lax.axis_index(axis)
    total = lax.dynamic_index_in_dim(x, me, 0, keepdims=False).astype(jnp.float32)
    for k in range(1, size):
        piece = lax.dynamic_index_in_dim(x, (me - k) % size, 0, keepdims=False)
        total = total + shifted(piece, axis, size, k).astype(jnp.float32)
    return total


def scatter_sum_paired(x, axis, size):
    me = lax.axis_index(axis)
    odd, group = me % 2, me // 2
    half = size // 2
    split = jnp.swapaxes(x.reshape((half, 2) + x.shape[1:]), 0, 1)
    mine = lax.dynamic_index_in_dim(split, odd, 0, keepdims=False).astype(jnp.float32)
    other = lax.dynamic_index_in_dim(split, 1 - odd, 0, keepdims=False)
    swapped = lax.ppermute(other, axis, [(j, j ^ 1) for j in range(size)])
    paired = (mine + swapped.astype(jnp.float32)).astype(jnp.bfloat16)
    total = lax.dynamic_index_in_dim(paired, group, 0, keepdims=False).astype(jnp.float32)
    for k in range(1, half):
        piece = lax.dynamic_index_in_dim(paired, (group - k) % half, 0, keepdims=False)
        total = total + shifted(piece, axis, size, 2 * k).astype(jnp.float32)
    return total


def scatter_sum_quad(x, zsize):
    zi, xi = lax.axis_index("z"), lax.axis_index("x_hi")
    odd, group = zi % 2, zi // 2
    half = zsize // 2
    four = x.reshape((half, 4) + x.shape[2:])
    total = lax.dynamic_index_in_dim(four, odd * 2 + xi, 1, keepdims=False).astype(jnp.float32)
    for flip_b, flip_x in ((1, 0), (0, 1), (1, 1)):
        other = jnp.where(flip_b == 1, 1 - odd, odd) * 2 + jnp.where(flip_x == 1, 1 - xi, xi)
        piece = lax.dynamic_index_in_dim(four, other, 1, keepdims=False)
        perm = [
            (xh * zsize + z, (xh ^ flip_x) * zsize + (z ^ flip_b))
            for xh in range(2)
            for z in range(zsize)
        ]
        total = total + lax.ppermute(piece, ("x_hi", "z"), perm).astype(jnp.float32)
    paired = total.astype(jnp.bfloat16)
    total = lax.dynamic_index_in_dim(paired, group, 0, keepdims=False).astype(jnp.float32)
    for k in range(1, half):
        piece = lax.dynamic_index_in_dim(paired, (group - k) % half, 0, keepdims=False)
        total = total + shifted(piece, "z", zsize, 2 * k).astype(jnp.float32)
    return total


def make_body(n_dp, owners):
    def per_device(tokens, grad_out, routes, gates, w_gate, w_up, w_down):
        local_count = w_gate.shape[0]
        experts_all = local_count * owners
        rows_dev, dmodel = tokens.shape
        dshard, hdim = w_gate.shape[1], w_gate.shape[2]
        hshard = w_down.shape[1]
        factor = jnp.float32((rows_dev * n_dp * owners) ** (-0.5))

        down_flat = w_down[0].reshape(dshard, hdim)
        packed = jnp.stack([w_gate[0], w_up[0], down_flat])
        gathered = gather_axis(packed, "x_hi", 2)
        gathered = gather_axis(gathered, "z", n_dp // 4)
        gathered = gather_axis(gathered, "core", 2)
        gathered = jnp.transpose(gathered, (2, 1, 0, 3, 4, 5))
        gathered = gathered.reshape((n_dp,) + packed.shape)
        gate_mat = gathered[:, 0].reshape(n_dp * dshard, hdim)
        up_mat = gathered[:, 1].reshape(n_dp * dshard, hdim)
        down_mat = gathered[:, 2].reshape(n_dp * hshard, dmodel)

        matched = routes[:, :, None] == jnp.arange(experts_all, dtype=jnp.int32)[None, None, :]
        chosen = jnp.any(matched, axis=1).astype(jnp.int32)
        weight_sel = jnp.sum(jnp.where(matched, gates[:, :, None], jnp.float32(0.0)), axis=1)
        slot = jnp.cumsum(chosen, axis=0) - 1
        slot_ids = jnp.arange(CAP, dtype=jnp.int32)
        place_mask = (slot.T[:, None, :] == slot_ids[None, :, None]) & (chosen.T[:, None, :] == 1)
        place_half = place_mask.astype(jnp.bfloat16)
        place_full = place_mask.astype(jnp.float32)
        gate_pick = jnp.einsum("ecr,re->ec", place_full, weight_sel, precision=lax.Precision.HIGHEST)
        pick_both = jnp.einsum(
            "ecr,rd->ecd",
            place_half,
            jnp.concatenate([tokens, grad_out], axis=1),
            preferred_element_type=jnp.float32,
        )
        scale = jnp.concatenate(
            [jnp.ones_like(gate_pick)[:, :, None] * jnp.ones((1, 1, dmodel), jnp.float32),
             gate_pick[:, :, None] * jnp.ones((1, 1, dmodel), jnp.float32)],
            axis=2,
        )
        both = lax.all_to_all(
            (scale * pick_both).astype(jnp.bfloat16), EX, split_axis=0, concat_axis=0, tiled=True
        )
        rows_in = both[:, :, :dmodel].reshape(owners * CAP, dmodel)
        grads_in = both[:, :, dmodel:].reshape(owners * CAP, dmodel)

        gate_value = jnp.dot(rows_in, gate_mat, preferred_element_type=jnp.float32)
        up_value = jnp.dot(rows_in, up_mat, preferred_element_type=jnp.float32)
        sigmoid_gate = jax.nn.sigmoid(gate_value)
        activated = gate_value * sigmoid_gate
        hidden = (activated * up_value).astype(jnp.bfloat16)
        d_hidden = contract_last(grads_in, down_mat)
        d_up = (d_hidden * activated).astype(jnp.bfloat16)
        d_gate = (
            d_hidden * up_value * sigmoid_gate * (1.0 + gate_value * (1.0 - sigmoid_gate))
        ).astype(jnp.bfloat16)

        gate_term = contract_first(rows_in, d_gate).astype(jnp.bfloat16)
        up_term = contract_first(rows_in, d_up).astype(jnp.bfloat16)
        down_term = contract_first(hidden, grads_in).astype(jnp.bfloat16)
        parts = jnp.stack(
            [
                gate_term.reshape(n_dp, dshard, hdim),
                up_term.reshape(n_dp, dshard, hdim),
                down_term.reshape(n_dp, dshard, hdim),
            ],
            axis=1,
        )
        parts = parts.reshape((2, n_dp // 4, 2) + parts.shape[1:])
        parts = jnp.transpose(parts, (2, 1, 0, 3, 4, 5))
        parts = scatter_sum_axis(parts, "core", 2).astype(jnp.bfloat16)
        d_rows = contract_last(d_gate, gate_mat) + contract_last(d_up, up_mat)
        back = d_rows.astype(jnp.bfloat16).reshape(owners, CAP, dmodel)
        parts, back = lax.optimization_barrier((parts, back))
        returned = lax.all_to_all(back, EX, split_axis=0, concat_axis=0, tiled=True)
        summed = scatter_sum_quad(parts, n_dp // 4)
        grad_gate = summed[0][None] * factor
        grad_up = summed[1][None] * factor
        grad_down = summed[2].reshape(1, hshard, dmodel) * factor

        grad_tokens = jnp.einsum(
            "ecr,ecd->rd", place_half, returned, preferred_element_type=jnp.float32
        ).astype(jnp.bfloat16)
        return (grad_tokens, grad_gate, grad_up, grad_down)

    return per_device


def solution(mesh):
    n_dp, owners = mesh.devices.shape
    fine = Mesh(
        np.asarray(mesh.devices).reshape(2, n_dp // 4, 2, owners // 2, 2),
        ("x_hi", "z", "core", "y", "x_lo"),
    )
    rows = P(DP + EX, None)
    weights = P(EX, DP, None)
    return jax.shard_map(
        make_body(n_dp, owners),
        mesh=fine,
        in_specs=(rows, rows, rows, rows, weights, weights, weights),
        out_specs=(rows, weights, weights, weights),
        check_vma=False,
    )
```
